128 devices in a mesh: ep: 32 (over z, x, core), tp: 4 (over y).
Axes of the slice: x: 4, y: 4, z: 4, core: 2. Of those that a mesh axis runs over, the one named last changes fastest.
Arguments:
- stream: bfloat16 [16384, 2048], P('ep'), may hold values from -6 to 6
- queries: bfloat16 [16384, 2048], P('ep', 'tp'), may hold values from -6 to 6
- keys_in: bfloat16 [16384, 2048], P('ep', 'tp'), may hold values from -6 to 6
- values_in: bfloat16 [16384, 2048], P('ep', 'tp'), may hold values from -6 to 6
- segment_ids: int32 [32, 512], P('ep'), may hold values from 0 to 5, never falling along the last dimension, each value on 1 to 256 neighbouring positions
- routes: int32 [16384, 4], P('ep'), may hold values from 0 to 63, all different within a row; in each aligned block of 512 rows (0 to 511, 512 to 1023, ...) at most 48 rows name the same one
- route_weights: float32 [16384, 4], P('ep'), may hold values from 0.1 to 0.6
- w_out: bfloat16 [2048, 2048], P('tp'), may hold values from -0.125 to 0.125
- norm_gain: float32 [2048], replicated, may hold values from 0.25 to 1.75
- expert_gate: bfloat16 [64, 2048, 1408], P('ep', None, 'tp'), may hold values from -0.125 to 0.125
- expert_up: bfloat16 [64, 2048, 1408], P('ep', None, 'tp'), may hold values from -0.125 to 0.125
- expert_down: bfloat16 [64, 1408, 2048], P('ep', 'tp'), may hold values from -0.15625 to 0.15625
- shared_gate: bfloat16 [2048, 3584], P(None, 'tp'), may hold values from -0.125 to 0.125
- shared_up: bfloat16 [2048, 3584], P(None, 'tp'), may hold values from -0.125 to 0.125
- shared_down: bfloat16 [3584, 2048], P('tp'), may hold values from -0.09375 to 0.09375
- shared_router: bfloat16 [2048], replicated, may hold values from -0.125 to 0.125
Outputs:
- mixed: bfloat16 [16384, 2048], P('ep', 'tp')
The draws below stay inside these ranges and needn't reach their ends.
Inputs may be any that keep to these rules, and one draw needn't show every extreme that they name: `routes`: in each aligned block of 512 rows, no expert is named by more than 48 rows, a bound that some block reaches. `segment_ids`: segment numbers never fall within a block; each prompt has at most 256 tokens, and some has exactly 256.
All inputs are finite; a program needn't handle non-finite values.
Results may differ from the reference program's by a relative error of at most 0.012.
Values may be sent and summed in bfloat16 or wider, within the bound.
No kernel may reach another device: no remote copies, remote signals or barrier semaphores. Data moves between devices by JAX's collectives and lax.ppermute only.
A program may use at most 128 MiB of HBM per device.

```python
import math
import jax
import jax.numpy as jnp
import numpy as np
from jax import lax

D = 2048
HEADS = 16
HEAD = 128
FF = 1408
TOPK = 4
SH = 3584
TOK_DEV = 512
SEGS = 6
SPAN = 256
EXPERTS = 64
CAP = 48
BLOCKS = 32
TOKENS = 16384
N_TP = 4


def drawn_part(key, salt):
    values = jnp.clip(jax.random.normal(jax.random.fold_in(key, salt), (TOKENS, D), jnp.float32), -5.5, 5.5)
    return values


def draw_queries(key, part):
    values = drawn_part(key, 21)
    return values.astype(jnp.bfloat16)


def draw_keys_in(key, part):
    values = drawn_part(key, 22)
    return values.astype(jnp.bfloat16)


def steps_of(key, extent, split, least, largest):
    level = 1.0
    for dim, parts in split:
        heights = jax.random.uniform(jax.random.fold_in(jax.random.fold_in(key, 6), dim), (parts,), jnp.float32, least / len(split), largest / len(split))
        level = level * jnp.repeat(jnp.exp(heights), extent[dim] // parts).reshape((-1,) + (1,) * (len(extent) - 1 - dim))
    return level


def split_up(number_of, total, bound, skew):
    weights = [(1 << 20) // math.isqrt(grade ** skew) + 1 for grade in range(2, number_of + 1)]
    spare, given = total - bound - (number_of - 1), [1] * (number_of - 1)
    while spare > 0:
        movable = [i for i in range(number_of - 1) if given[i] < bound]
        pool, left = sum([weights[i] for i in movable]), spare
        for i in movable:
            addition = min(bound - given[i], max(1, left * weights[i] // pool), spare)
            given[i] = given[i] + addition
            spare = spare - addition
    return np.array([bound] + given)


def ragged_sizes(key, amount, total, bound, slope):
    if amount == 2:
        one = jax.random.randint(key, (), max(1, total - bound), min(bound, total - 1) + 1)
        return jnp.stack([one, total - one])
    tallies = jnp.asarray(split_up(amount, total, bound, slope), jnp.int32)
    pairs = (amount - 1) // 2
    source_of, sink = tallies[1:1 + 2 * pairs:2], tallies[2:2 + 2 * pairs:2]
    room = jnp.minimum(source_of - 1, bound - sink)
    passed = jax.random.randint(jax.random.fold_in(key, 1), (pairs,), 0, 1 << 20) % (room + 1)
    tallies = tallies.at[1:1 + 2 * pairs:2].set(source_of - passed).at[2:2 + 2 * pairs:2].set(sink + passed)
    return tallies[jax.random.permutation(jax.random.fold_in(key, 2), amount)]


def routed_block(key, own, number, rows, number_of, top, limit, lean):
    sequence = jax.random.permutation(key, number_of)
    packed, common = load_shares(number_of, rows * top, limit, lean, True), load_shares(number_of, rows * top, limit, lean, False)
    places = jnp.arange(number_of)

    def named(tallies, rotation):
        used = int((tallies > 0).sum())
        fixed = max(1, used // 4)
        shifted = fixed + (places - fixed + rotation * (used - fixed)) % max(1, number_of - fixed)
        return jnp.zeros((number_of,), jnp.int32).at[sequence[jnp.where(places < fixed, places, shifted)]].set(jnp.asarray(tallies, jnp.int32))

    tallies = jnp.where(number % 4 == 0, named(packed, number // 4), named(common, number - number // 4 - 1))
    mixed = jax.random.permutation(jax.random.fold_in(own, 3), number_of)
    giver, receiver = mixed[0:number_of // 2 * 2:2], mixed[1:number_of // 2 * 2:2]
    margin = jnp.minimum(tallies[giver] - 1, limit - tallies[receiver]) // 2
    margin = jnp.where((giver == sequence[0]) | (receiver == sequence[0]) | (tallies[receiver] == 0), 0, jnp.maximum(margin, 0))
    shifted = jax.random.randint(jax.random.fold_in(own, 4), (number_of // 2,), 0, 1 << 20) % (margin + 1)
    tallies = tallies.at[giver].add(-shifted).at[receiver].add(shifted)
    items = jnp.searchsorted(jnp.cumsum(tallies), jnp.arange(rows * top), side="right").astype(jnp.int32)
    table = items.reshape(top, rows).T
    table = table[jax.random.permutation(jax.random.fold_in(own, 1), rows)]
    rotation = jax.random.randint(jax.random.fold_in(own, 2), (rows, 1), 0, top)
    return jnp.take_along_axis(table, (jnp.arange(top)[None, :] + rotation) % top, axis=1)


def load_shares(amount, total, reach, slope, full):
    loads = [(1 << 20) // math.isqrt(rank ** slope) + 1 for rank in range(1, amount + 1)]
    largest = reach if full else min(reach, max(-(-total // amount), total * loads[0] // sum(loads)))
    least = 1 if total - largest >= amount - 1 else 0
    given, surplus = [largest] + [least] * (amount - 1), total - largest - least * (amount - 1)
    while surplus > 0:
        movable = [i for i in range(1, amount) if given[i] < largest] or [i for i in range(1, amount) if given[i] < reach]
        pool, remaining = sum([loads[i] for i in movable]), surplus
        for i in movable:
            extra = min(reach - given[i], max(1, remaining * loads[i] // pool), surplus)
            given[i] = given[i] + extra
            surplus = surplus - extra
    return np.array(given)


def noise(stream_key, shape, scale, most, split=(), kind=jnp.bfloat16):
    level = steps_of(stream_key, shape, split, -0.22, 0.18) if split else 1.0
    entries = jax.random.normal(stream_key, shape, jnp.float32) * scale * level
    return jnp.minimum(jnp.maximum(entries, -most), most).astype(kind)


def setup_inputs(seed: int = 0) -> dict:
    seeds = jax.random.split(jax.random.key(seed), 17)
    stream = noise(seeds[0], (TOKENS, D), 1.0, 6.0, ((0, 32),))
    queries = draw_queries(jax.random.fold_in(seeds[16], 71), 0)
    keys_in = draw_keys_in(jax.random.fold_in(seeds[16], 71), 0)
    values_in = noise(seeds[3], (TOKENS, D), 1.0, 6.0, ((0, 32), (1, 4)))
    segment_ids = jax.vmap(lambda own: jnp.searchsorted(jnp.cumsum(ragged_sizes(own, SEGS, TOK_DEV, SPAN, 2)), jnp.arange(TOK_DEV), side="right"))(jax.random.split(seeds[4], BLOCKS)).reshape((BLOCKS, TOK_DEV)).astype(jnp.int32)
    routes_keys = jax.random.split(jax.random.fold_in(seeds[5], 1), TOKENS // TOK_DEV)
    routes_turns = jax.random.permutation(jax.random.fold_in(seeds[5], 3), TOKENS // TOK_DEV)
    routes = jax.vmap(lambda own, number: routed_block(jax.random.fold_in(seeds[5], 2), own, number, TOK_DEV, EXPERTS, TOPK, CAP, 2))(routes_keys, routes_turns).reshape((TOKENS, TOPK))
    route_weights = jnp.clip(0.1 + 0.5 * jax.random.uniform(seeds[6], (TOKENS, TOPK), jnp.float32) ** steps_of(seeds[6], (TOKENS, TOPK), ((0, 32),), -0.2, 0.2), 0.1, 0.6)
    w_out = noise(seeds[7], (D, D), D ** -0.5, 0.125, ((0, 4),))
    norm_gain = jnp.clip(1.0 + 0.15 * jax.random.normal(seeds[8], (D,), jnp.float32), 0.25, 1.75)
    expert_gate = noise(seeds[9], (EXPERTS, D, FF), D ** -0.5, 0.125, ((0, 32), (2, 4)))
    expert_up = noise(seeds[10], (EXPERTS, D, FF), D ** -0.5, 0.125, ((0, 32), (2, 4)))
    expert_down = noise(seeds[11], (EXPERTS, FF, D), FF ** -0.5, 0.15625, ((0, 32), (1, 4)))
    shared_gate = noise(seeds[12], (D, SH), D ** -0.5, 0.125, ((1, 4),))
    shared_up = noise(seeds[13], (D, SH), D ** -0.5, 0.125, ((1, 4),))
    shared_down = noise(seeds[14], (SH, D), SH ** -0.5, 0.09375, ((0, 4),))
    shared_router = noise(seeds[15], (D,), D ** -0.5, 0.125)
    return dict(stream=stream, queries=queries, keys_in=keys_in, values_in=values_in, segment_ids=segment_ids, routes=routes, route_weights=route_weights, w_out=w_out, norm_gain=norm_gain, expert_gate=expert_gate, expert_up=expert_up, expert_down=expert_down, shared_gate=shared_gate, shared_up=shared_up, shared_down=shared_down, shared_router=shared_router)


def slots_of(block_routes, experts, capacity):
    length, picks = block_routes.shape
    flat = block_routes.reshape(length * picks).astype(jnp.int32)
    onehot = (flat[:, None] == jnp.arange(experts, dtype=jnp.int32)[None, :]).astype(jnp.int32)
    before = jnp.cumsum(onehot, axis=0, dtype=jnp.int32) - onehot
    rank = lax.optimization_barrier(jnp.sum(before * onehot, axis=1, dtype=jnp.int32))
    slot = (flat * capacity + rank).astype(jnp.int32)
    owners = (jnp.arange(length * picks, dtype=jnp.int32) // picks).astype(jnp.int32)
    table = jnp.full((experts * capacity,), -1, dtype=jnp.int32).at[slot].set(owners)
    return (slot.reshape(length, picks), table)

def attend_block(operands):
    query_block, key_block, value_block, segment = operands
    length = query_block.shape[0]
    query_heads = query_block.astype(jnp.float32).reshape(length, HEADS, HEAD)
    key_heads = key_block.astype(jnp.float32).reshape(length, HEADS, HEAD)
    value_heads = value_block.astype(jnp.float32).reshape(length, HEADS, HEAD)
    places = jnp.arange(length, dtype=jnp.int32)
    allowed = (segment[:, None] == segment[None, :]) & (places[:, None] >= places[None, :])
    scores = jnp.einsum('qhd,khd->hqk', query_heads, key_heads) * HEAD ** (-0.5)
    scores = jnp.where(allowed[None], scores, -jnp.inf)
    highest = lax.optimization_barrier(jnp.max(scores, axis=2, keepdims=True))
    weights = jnp.exp(scores - highest)
    shares = (weights / lax.optimization_barrier(jnp.sum(weights, axis=2, keepdims=True))).astype(jnp.bfloat16)
    attended = jnp.einsum('hqk,khd->qhd', shares.astype(jnp.float32), value_heads)
    return attended.astype(jnp.bfloat16).reshape(length, D)

def grouped_down(hidden, down, groups):
    width = hidden.shape[1] // groups
    total = jnp.zeros((hidden.shape[0], down.shape[1]), jnp.float32)
    for index in range(groups):
        piece = jnp.dot(hidden[:, index * width:(index + 1) * width], down[index * width:(index + 1) * width], preferred_element_type=jnp.float32)
        total = total + lax.optimization_barrier(piece.astype(jnp.bfloat16)).astype(jnp.float32)
    return total

def reference(stream, queries, keys_in, values_in, segment_ids, routes, route_weights, w_out, norm_gain, expert_gate, expert_up, expert_down, shared_gate, shared_up, shared_down, shared_router):
    blocks, length = segment_ids.shape
    attended = lax.map(attend_block, (queries.reshape(blocks, length, D), keys_in.reshape(blocks, length, D), values_in.reshape(blocks, length, D), segment_ids))
    attended = attended.reshape(blocks * length, D)
    resid = stream.astype(jnp.float32) + jnp.dot(attended, w_out, preferred_element_type=jnp.float32)
    normed = (resid * lax.rsqrt(lax.optimization_barrier(jnp.mean(resid * resid, axis=1, keepdims=True)) + 1e-06) * norm_gain).astype(jnp.bfloat16)

    def shared_block(rows):
        gate = jnp.dot(rows, shared_gate, preferred_element_type=jnp.float32)
        upward = jnp.dot(rows, shared_up, preferred_element_type=jnp.float32)
        hidden = (jax.nn.silu(gate) * upward).astype(jnp.bfloat16)
        return grouped_down(hidden, shared_down, N_TP)
    shared_out = lax.map(shared_block, normed.reshape(blocks, length, D)).reshape(blocks * length, D)
    shared_scale = jax.nn.sigmoid(jnp.dot(normed, shared_router, preferred_element_type=jnp.float32))
    slot, table = jax.vmap(lambda block_routes: slots_of(block_routes, EXPERTS, CAP))(routes.reshape(blocks, length, TOPK))
    offsets = (jnp.arange(blocks, dtype=jnp.int32) * length)[:, None]

    def run_expert(index):
        ids = lax.dynamic_slice_in_dim(table, (index * CAP).astype(jnp.int32), CAP, 1)
        live = (ids >= 0).reshape(-1)
        rows = jnp.take(normed, (jnp.maximum(ids, 0) + offsets).reshape(-1).astype(jnp.int32), axis=0)
        rows = jnp.where(live[:, None], rows, jnp.zeros_like(rows))
        gate = jnp.dot(rows, expert_gate[index], preferred_element_type=jnp.float32)
        upward = jnp.dot(rows, expert_up[index], preferred_element_type=jnp.float32)
        hidden = (jax.nn.silu(gate) * upward).astype(jnp.bfloat16)
        return grouped_down(hidden, expert_down[index], N_TP).astype(jnp.bfloat16)
    results = lax.map(run_expert, jnp.arange(EXPERTS, dtype=jnp.int32)).reshape(EXPERTS * blocks * CAP, D)
    expert_of = slot // CAP
    rank = slot % CAP
    where_row = (expert_of * (blocks * CAP) + jnp.arange(blocks, dtype=jnp.int32)[:, None, None] * CAP + rank).reshape(blocks * length, TOPK).astype(jnp.int32)
    routed = jnp.zeros((blocks * length, D), jnp.float32)
    for choice_index in range(TOPK):
        picked = jnp.take(results, where_row[:, choice_index], axis=0).astype(jnp.float32)
        routed = routed + route_weights[:, choice_index][:, None] * picked
    return (resid + shared_scale[:, None] * shared_out + routed).astype(jnp.bfloat16)
```

```python
import jax
import jax.numpy as jnp
from jax import lax
from jax.sharding import PartitionSpec as P

HEAD = 128


def slots_of(block_routes, experts, capacity):
    length, picks = block_routes.shape
    count = length * picks
    flat = block_routes.reshape(count)
    onehot = flat[:, None] == jnp.arange(experts, dtype=jnp.int32)[None, :]
    places = jnp.arange(count, dtype=jnp.int32)
    earlier = (places[:, None] > places[None, :]).astype(jnp.bfloat16)
    before = jnp.dot(earlier, onehot.astype(jnp.bfloat16), preferred_element_type=jnp.float32)
    rank = jnp.sum(jnp.where(onehot, before, 0.0), axis=1).astype(jnp.int32)
    slot = flat * capacity + rank
    return slot.reshape(length, picks)


def attend_local(query_block, key_block, value_block, segment):
    length = query_block.shape[0]
    heads = query_block.shape[1] // HEAD
    places = jnp.arange(length, dtype=jnp.int32)
    allowed = (segment[:, None] == segment[None, :]) & (places[:, None] >= places[None, :])

    def one_head(operands):
        query_rows, key_rows, value_rows = operands
        scores = jnp.dot(query_rows, key_rows.T, preferred_element_type=jnp.float32) * HEAD ** (
            -0.5
        )
        scores = jnp.where(allowed, scores, -jnp.inf)
        highest = jnp.max(scores, axis=1, keepdims=True)
        weights = jnp.exp(scores - highest)
        shares = (weights / jnp.sum(weights, axis=1, keepdims=True)).astype(jnp.bfloat16)
        return jnp.dot(shares, value_rows, preferred_element_type=jnp.float32).astype(jnp.bfloat16)

    def by_head(values):
        return values.reshape(length, heads, HEAD).transpose(1, 0, 2)

    attended = lax.map(one_head, (by_head(query_block), by_head(key_block), by_head(value_block)))
    return attended.transpose(1, 0, 2).reshape(length, heads * HEAD)


def on_device(
    stream,
    queries,
    keys_in,
    values_in,
    segment_ids,
    routes,
    route_weights,
    w_out,
    norm_gain,
    expert_gate,
    expert_up,
    expert_down,
    shared_gate,
    shared_up,
    shared_down,
    shared_router,
):
    length, width = stream.shape
    ep_count = lax.axis_size("ep")
    tp_count = lax.axis_size("tp")
    attended = attend_local(queries, keys_in, values_in, segment_ids[0])
    partial_value = jnp.dot(attended, w_out, preferred_element_type=jnp.float32)
    resid = stream.astype(jnp.float32) + lax.psum(partial_value.astype(jnp.bfloat16), "tp").astype(
        jnp.float32
    )
    normed = (
        resid * lax.rsqrt(jnp.mean(resid * resid, axis=1, keepdims=True) + 1e-06) * norm_gain
    ).astype(jnp.bfloat16)
    shared_gate_rows = jnp.dot(normed, shared_gate, preferred_element_type=jnp.float32)
    shared_up_rows = jnp.dot(normed, shared_up, preferred_element_type=jnp.float32)
    shared_hidden = (jax.nn.silu(shared_gate_rows) * shared_up_rows).astype(jnp.bfloat16)
    shared_part = jnp.dot(shared_hidden, shared_down, preferred_element_type=jnp.float32)
    shared_cols = lax.psum_scatter(
        shared_part.astype(jnp.bfloat16), "tp", scatter_dimension=1, tiled=True
    ).astype(jnp.float32)
    shared_scale = jax.nn.sigmoid(
        jnp.dot(normed, shared_router, preferred_element_type=jnp.float32)
    )
    local_experts = expert_gate.shape[0]
    experts = local_experts * ep_count
    picks = routes.shape[1]
    divisor = 2 * experts * tp_count
    capacity = tp_count * ((3 * length * picks + divisor - 1) // divisor)
    slot = slots_of(routes, experts, capacity)
    slot_ids = jnp.arange(experts * capacity, dtype=jnp.int32)
    hits = slot[:, :, None] == slot_ids[None, None, :]
    chosen = jnp.any(hits, axis=1).T.astype(jnp.bfloat16)
    outgoing = jnp.dot(chosen, normed, preferred_element_type=jnp.float32).astype(jnp.bfloat16)
    outgoing = outgoing.reshape(ep_count, local_experts, capacity, width)
    incoming = lax.all_to_all(outgoing, "ep", split_axis=0, concat_axis=0, tiled=True)
    gate_rows = jnp.einsum(
        "sjcd,jdf->sjcf", incoming, expert_gate, preferred_element_type=jnp.float32
    )
    up_rows = jnp.einsum("sjcd,jdf->sjcf", incoming, expert_up, preferred_element_type=jnp.float32)
    expert_hidden = (jax.nn.silu(gate_rows) * up_rows).astype(jnp.bfloat16)
    expert_part = jnp.einsum(
        "sjcf,jfd->sjcd", expert_hidden, expert_down, preferred_element_type=jnp.float32
    )
    expert_cols = lax.psum_scatter(
        expert_part.astype(jnp.bfloat16), "tp", scatter_dimension=3, tiled=True
    )
    returned = lax.all_to_all(expert_cols, "ep", split_axis=0, concat_axis=0, tiled=True)
    columns = returned.shape[3]
    flat_results = returned.reshape(experts * capacity, columns)
    mixing = jnp.sum(jnp.where(hits, route_weights[:, :, None], 0.0), axis=1)
    mixing_high = mixing.astype(jnp.bfloat16)
    mixing_low = (mixing - mixing_high.astype(jnp.float32)).astype(jnp.bfloat16)
    routed = jnp.dot(mixing_high, flat_results, preferred_element_type=jnp.float32) + jnp.dot(
        mixing_low, flat_results, preferred_element_type=jnp.float32
    )
    resid_cols = lax.dynamic_slice_in_dim(resid, lax.axis_index("tp") * columns, columns, 1)
    return (resid_cols + shared_scale[:, None] * shared_cols + routed).astype(jnp.bfloat16)


def solution(mesh):
    placed = (
        P("ep", None),
        P("ep", "tp"),
        P("ep", "tp"),
        P("ep", "tp"),
        P("ep", None),
        P("ep", None),
        P("ep", None),
        P("tp", None),
        P(),
        P("ep", None, "tp"),
        P("ep", None, "tp"),
        P("ep", "tp", None),
        P(None, "tp"),
        P(None, "tp"),
        P("tp", None),
        P(),
    )
    return jax.shard_map(
        on_device, mesh=mesh, in_specs=placed, out_specs=P("ep", "tp"), check_vma=False
    )
```

```python
import jax
import jax.numpy as jnp
from jax import lax
from jax.sharding import PartitionSpec as P

HEAD = 128


def slots_of(block_routes, experts, capacity):
    length, picks = block_routes.shape
    count = length * picks
    flat = block_routes.reshape(count)
    onehot = flat[:, None] == jnp.arange(experts, dtype=jnp.int32)[None, :]
    places = jnp.arange(count, dtype=jnp.int32)
    earlier = (places[:, None] > places[None, :]).astype(jnp.bfloat16)
    before = jnp.dot(earlier, onehot.astype(jnp.bfloat16), preferred_element_type=jnp.float32)
    rank = jnp.sum(jnp.where(onehot, before, 0.0), axis=1).astype(jnp.int32)
    slot = flat * capacity + rank
    return slot.reshape(length, picks)


def attend_local(query_block, key_block, value_block, segment):
    length = query_block.shape[0]
    heads = query_block.shape[1] // HEAD
    places = jnp.arange(length, dtype=jnp.int32)
    allowed = (segment[:, None] == segment[None, :]) & (places[:, None] >= places[None, :])

    def one_head(operands):
        query_rows, key_rows, value_rows = operands
        scores = jnp.dot(query_rows, key_rows.T, preferred_element_type=jnp.float32) * HEAD ** (
            -0.5
        )
        scores = jnp.where(allowed, scores, -jnp.inf)
        highest = jnp.max(scores, axis=1, keepdims=True)
        weights = jnp.exp(scores - highest)
        shares = (weights / jnp.sum(weights, axis=1, keepdims=True)).astype(jnp.bfloat16)
        return jnp.dot(shares, value_rows, preferred_element_type=jnp.float32).astype(jnp.bfloat16)

    def by_head(values):
        return values.reshape(length, heads, HEAD).transpose(1, 0, 2)

    attended = lax.map(one_head, (by_head(query_block), by_head(key_block), by_head(value_block)))
    return attended.transpose(1, 0, 2).reshape(length, heads * HEAD)


def on_device(
    stream,
    queries,
    keys_in,
    values_in,
    segment_ids,
    routes,
    route_weights,
    w_out,
    norm_gain,
    expert_gate,
    expert_up,
    expert_down,
    shared_gate,
    shared_up,
    shared_down,
    shared_router,
):
    length, width = stream.shape
    ep_count = lax.axis_size("ep")
    tp_count = lax.axis_size("tp")
    attended = attend_local(queries, keys_in, values_in, segment_ids[0])
    partial_value = jnp.dot(attended, w_out, preferred_element_type=jnp.float32)
    resid = stream.astype(jnp.float32) + lax.psum(partial_value.astype(jnp.bfloat16), "tp").astype(
        jnp.float32
    )
    normed = (
        resid * lax.rsqrt(jnp.mean(resid * resid, axis=1, keepdims=True) + 1e-06) * norm_gain
    ).astype(jnp.bfloat16)
    shared_gate_rows = jnp.dot(normed, shared_gate, preferred_element_type=jnp.float32)
    shared_up_rows = jnp.dot(normed, shared_up, preferred_element_type=jnp.float32)
    shared_hidden = (jax.nn.silu(shared_gate_rows) * shared_up_rows).astype(jnp.bfloat16)
    shared_part = jnp.dot(shared_hidden, shared_down, preferred_element_type=jnp.float32)
    shared_cols = lax.psum_scatter(
        shared_part.astype(jnp.bfloat16), "tp", scatter_dimension=1, tiled=True
    ).astype(jnp.float32)
    shared_scale = jax.nn.sigmoid(
        jnp.dot(normed, shared_router, preferred_element_type=jnp.float32)
    )
    local_experts = expert_gate.shape[0]
    experts = local_experts * ep_count
    picks = routes.shape[1]
    divisor = 2 * experts * tp_count
    capacity = tp_count * ((3 * length * picks + divisor - 1) // divisor)
    slot = slots_of(routes, experts, capacity)
    slot_ids = jnp.arange(experts * capacity, dtype=jnp.int32)
    hits = slot[:, :, None] == slot_ids[None, None, :]
    chosen = jnp.any(hits, axis=1).T.astype(jnp.bfloat16)
    chosen = chosen.reshape(ep_count, local_experts, capacity, length)
    chunks = 4 if capacity % 4 == 0 else 1
    step = capacity // chunks
    pieces = []
    for index in range(chunks):
        picks_of = chosen[:, :, index * step : (index + 1) * step]
        outgoing = jnp.einsum(
            "sjct,td->sjcd", picks_of, normed, preferred_element_type=jnp.float32
        ).astype(jnp.bfloat16)
        incoming = lax.all_to_all(outgoing, "ep", split_axis=0, concat_axis=0, tiled=True)
        gate_rows = jnp.einsum(
            "sjcd,jdf->sjcf", incoming, expert_gate, preferred_element_type=jnp.float32
        )
        up_rows = jnp.einsum(
            "sjcd,jdf->sjcf", incoming, expert_up, preferred_element_type=jnp.float32
        )
        expert_hidden = (jax.nn.silu(gate_rows) * up_rows).astype(jnp.bfloat16)
        expert_part = jnp.einsum(
            "sjcf,jfd->sjcd", expert_hidden, expert_down, preferred_element_type=jnp.float32
        )
        expert_cols = lax.psum_scatter(
            expert_part.astype(jnp.bfloat16), "tp", scatter_dimension=3, tiled=True
        )
        pieces.append(lax.all_to_all(expert_cols, "ep", split_axis=0, concat_axis=0, tiled=True))
    returned = jnp.concatenate(pieces, axis=2)
    columns = returned.shape[3]
    flat_results = returned.reshape(experts * capacity, columns)
    mixing = jnp.sum(jnp.where(hits, route_weights[:, :, None], 0.0), axis=1)
    mixing_high = mixing.astype(jnp.bfloat16)
    mixing_low = (mixing - mixing_high.astype(jnp.float32)).astype(jnp.bfloat16)
    routed = jnp.dot(mixing_high, flat_results, preferred_element_type=jnp.float32) + jnp.dot(
        mixing_low, flat_results, preferred_element_type=jnp.float32
    )
    resid_cols = lax.dynamic_slice_in_dim(resid, lax.axis_index("tp") * columns, columns, 1)
    return (resid_cols + shared_scale[:, None] * shared_cols + routed).astype(jnp.bfloat16)


def solution(mesh):
    placed = (
        P("ep", None),
        P("ep", "tp"),
        P("ep", "tp"),
        P("ep", "tp"),
        P("ep", None),
        P("ep", None),
        P("ep", None),
        P("tp", None),
        P(),
        P("ep", None, "tp"),
        P("ep", None, "tp"),
        P("ep", "tp", None),
        P(None, "tp"),
        P(None, "tp"),
        P("tp", None),
        P(),
    )
    return jax.shard_map(
        on_device, mesh=mesh, in_specs=placed, out_specs=P("ep", "tp"), check_vma=False
    )
```

```python
import jax
import jax.numpy as jnp
from jax import lax
from jax.sharding import PartitionSpec as P

HEAD = 128


def slots_of(block_routes, experts, capacity):
    length, picks = block_routes.shape
    count = length * picks
    flat = block_routes.reshape(count)
    onehot = flat[:, None] == jnp.arange(experts, dtype=jnp.int32)[None, :]
    places = jnp.arange(count, dtype=jnp.int32)
    earlier = (places[:, None] > places[None, :]).astype(jnp.bfloat16)
    before = jnp.dot(earlier, onehot.astype(jnp.bfloat16), preferred_element_type=jnp.float32)
    rank = jnp.sum(jnp.where(onehot, before, 0.0), axis=1).astype(jnp.int32)
    slot = flat * capacity + rank
    return slot.reshape(length, picks)


def attend_local(query_block, key_block, value_block, segment):
    length = query_block.shape[0]
    heads = query_block.shape[1] // HEAD
    places = jnp.arange(length, dtype=jnp.int32)
    allowed = (segment[:, None] == segment[None, :]) & (places[:, None] >= places[None, :])

    def one_head(operands):
        query_rows, key_rows, value_rows = operands
        scores = jnp.dot(query_rows, key_rows.T, preferred_element_type=jnp.float32) * HEAD ** (
            -0.5
        )
        scores = jnp.where(allowed, scores, -jnp.inf)
        highest = jnp.max(scores, axis=1, keepdims=True)
        weights = jnp.exp(scores - highest)
        shares = (weights / jnp.sum(weights, axis=1, keepdims=True)).astype(jnp.bfloat16)
        return jnp.dot(shares, value_rows, preferred_element_type=jnp.float32).astype(jnp.bfloat16)

    def by_head(values):
        return values.reshape(length, heads, HEAD).transpose(1, 0, 2)

    attended = lax.map(one_head, (by_head(query_block), by_head(key_block), by_head(value_block)))
    return attended.transpose(1, 0, 2).reshape(length, heads * HEAD)


def on_device(
    stream,
    queries,
    keys_in,
    values_in,
    segment_ids,
    routes,
    route_weights,
    w_out,
    norm_gain,
    expert_gate,
    expert_up,
    expert_down,
    shared_gate,
    shared_up,
    shared_down,
    shared_router,
):
    length, width = stream.shape
    ep_count = lax.axis_size("ep")
    tp_count = lax.axis_size("tp")
    attended = attend_local(queries, keys_in, values_in, segment_ids[0])
    partial_value = jnp.dot(attended, w_out, preferred_element_type=jnp.float32)
    resid = stream.astype(jnp.float32) + lax.psum(partial_value.astype(jnp.bfloat16), "tp").astype(
        jnp.float32
    )
    normed = (
        resid * lax.rsqrt(jnp.mean(resid * resid, axis=1, keepdims=True) + 1e-06) * norm_gain
    ).astype(jnp.bfloat16)
    shared_gate_rows = jnp.dot(normed, shared_gate, preferred_element_type=jnp.float32)
    shared_up_rows = jnp.dot(normed, shared_up, preferred_element_type=jnp.float32)
    shared_hidden = (jax.nn.silu(shared_gate_rows) * shared_up_rows).astype(jnp.bfloat16)
    shared_part = jnp.dot(shared_hidden, shared_down, preferred_element_type=jnp.float32)
    shared_cols = lax.psum_scatter(
        shared_part.astype(jnp.bfloat16), "tp", scatter_dimension=1, tiled=True
    ).astype(jnp.float32)
    shared_scale = jax.nn.sigmoid(
        jnp.dot(normed, shared_router, preferred_element_type=jnp.float32)
    )
    local_experts = expert_gate.shape[0]
    experts = local_experts * ep_count
    picks = routes.shape[1]
    divisor = 2 * experts * tp_count
    capacity = tp_count * ((3 * length * picks + divisor - 1) // divisor)
    slot = slots_of(routes, experts, capacity)
    slot_ids = jnp.arange(experts * capacity, dtype=jnp.int32)
    hits = slot[:, :, None] == slot_ids[None, None, :]
    chosen = jnp.any(hits, axis=1).T.astype(jnp.bfloat16)
    outgoing = jnp.dot(chosen, normed, preferred_element_type=jnp.float32).astype(jnp.bfloat16)
    outgoing = outgoing.reshape(ep_count, local_experts, capacity, width)
    incoming = lax.all_to_all(outgoing, "ep", split_axis=0, concat_axis=0, tiled=True)
    chunks = 4 if capacity % 4 == 0 else 1
    step = capacity // chunks
    pieces = []
    for index in range(chunks):
        rows = incoming[:, :, index * step : (index + 1) * step]
        gate_rows = jnp.einsum(
            "sjcd,jdf->sjcf", rows, expert_gate, preferred_element_type=jnp.float32
        )
        up_rows = jnp.einsum("sjcd,jdf->sjcf", rows, expert_up, preferred_element_type=jnp.float32)
        expert_hidden = (jax.nn.silu(gate_rows) * up_rows).astype(jnp.bfloat16)
        expert_part = jnp.einsum(
            "sjcf,jfd->sjcd", expert_hidden, expert_down, preferred_element_type=jnp.float32
        )
        expert_cols = lax.psum_scatter(
            expert_part.astype(jnp.bfloat16), "tp", scatter_dimension=3, tiled=True
        )
        pieces.append(lax.all_to_all(expert_cols, "ep", split_axis=0, concat_axis=0, tiled=True))
    returned = jnp.concatenate(pieces, axis=2)
    columns = returned.shape[3]
    flat_results = returned.reshape(experts * capacity, columns)
    mixing = jnp.sum(jnp.where(hits, route_weights[:, :, None], 0.0), axis=1)
    mixing_high = mixing.astype(jnp.bfloat16)
    mixing_low = (mixing - mixing_high.astype(jnp.float32)).astype(jnp.bfloat16)
    routed = jnp.dot(mixing_high, flat_results, preferred_element_type=jnp.float32) + jnp.dot(
        mixing_low, flat_results, preferred_element_type=jnp.float32
    )
    resid_cols = lax.dynamic_slice_in_dim(resid, lax.axis_index("tp") * columns, columns, 1)
    return (resid_cols + shared_scale[:, None] * shared_cols + routed).astype(jnp.bfloat16)


def solution(mesh):
    placed = (
        P("ep", None),
        P("ep", "tp"),
        P("ep", "tp"),
        P("ep", "tp"),
        P("ep", None),
        P("ep", None),
        P("ep", None),
        P("tp", None),
        P(),
        P("ep", None, "tp"),
        P("ep", None, "tp"),
        P("ep", "tp", None),
        P(None, "tp"),
        P(None, "tp"),
        P("tp", None),
        P(),
    )
    return jax.shard_map(
        on_device, mesh=mesh, in_specs=placed, out_specs=P("ep", "tp"), check_vma=False
    )
```

```python
import jax
import jax.numpy as jnp
from jax import lax
from jax.sharding import PartitionSpec as P

HEAD = 128


def slots_of(block_routes, experts, capacity):
    length, picks = block_routes.shape
    count = length * picks
    flat = block_routes.reshape(count)
    onehot = flat[:, None] == jnp.arange(experts, dtype=jnp.int32)[None, :]
    places = jnp.arange(count, dtype=jnp.int32)
    earlier = (places[:, None] > places[None, :]).astype(jnp.bfloat16)
    before = jnp.dot(earlier, onehot.astype(jnp.bfloat16), preferred_element_type=jnp.float32)
    rank = jnp.sum(jnp.where(onehot, before, 0.0), axis=1).astype(jnp.int32)
    slot = flat * capacity + rank
    return slot.reshape(length, picks)


def attend_local(query_block, key_block, value_block, segment):
    length = query_block.shape[0]
    heads = query_block.shape[1] // HEAD
    places = jnp.arange(length, dtype=jnp.int32)
    allowed = (segment[:, None] == segment[None, :]) & (places[:, None] >= places[None, :])

    def one_head(operands):
        query_rows, key_rows, value_rows = operands
        scores = jnp.dot(query_rows, key_rows.T, preferred_element_type=jnp.float32) * HEAD ** (
            -0.5
        )
        scores = jnp.where(allowed, scores, -jnp.inf)
        highest = jnp.max(scores, axis=1, keepdims=True)
        weights = jnp.exp(scores - highest)
        shares = (weights / jnp.sum(weights, axis=1, keepdims=True)).astype(jnp.bfloat16)
        return jnp.dot(shares, value_rows, preferred_element_type=jnp.float32).astype(jnp.bfloat16)

    def by_head(values):
        return values.reshape(length, heads, HEAD).transpose(1, 0, 2)

    attended = lax.map(one_head, (by_head(query_block), by_head(key_block), by_head(value_block)))
    return attended.transpose(1, 0, 2).reshape(length, heads * HEAD)


def on_device(
    stream,
    queries,
    keys_in,
    values_in,
    segment_ids,
    routes,
    route_weights,
    w_out,
    norm_gain,
    expert_gate,
    expert_up,
    expert_down,
    shared_gate,
    shared_up,
    shared_down,
    shared_router,
):
    length, width = stream.shape
    ep_count = lax.axis_size("ep")
    tp_count = lax.axis_size("tp")
    attended = attend_local(queries, keys_in, values_in, segment_ids[0])
    partial_value = jnp.dot(attended, w_out, preferred_element_type=jnp.float32)
    resid = stream.astype(jnp.float32) + lax.psum(partial_value.astype(jnp.bfloat16), "tp").astype(
        jnp.float32
    )
    normed = (
        resid * lax.rsqrt(jnp.mean(resid * resid, axis=1, keepdims=True) + 1e-06) * norm_gain
    ).astype(jnp.bfloat16)
    shared_gate_rows = jnp.dot(normed, shared_gate, preferred_element_type=jnp.float32)
    shared_up_rows = jnp.dot(normed, shared_up, preferred_element_type=jnp.float32)
    shared_hidden = (jax.nn.silu(shared_gate_rows) * shared_up_rows).astype(jnp.bfloat16)
    shared_part = jnp.dot(shared_hidden, shared_down, preferred_element_type=jnp.float32)
    shared_cols = lax.psum_scatter(
        shared_part.astype(jnp.bfloat16), "tp", scatter_dimension=1, tiled=True
    ).astype(jnp.float32)
    shared_scale = jax.nn.sigmoid(
        jnp.dot(normed, shared_router, preferred_element_type=jnp.float32)
    )
    local_experts = expert_gate.shape[0]
    experts = local_experts * ep_count
    picks = routes.shape[1]
    divisor = 2 * experts * tp_count
    capacity = tp_count * ((3 * length * picks + divisor - 1) // divisor)
    slot = slots_of(routes, experts, capacity)
    slot_ids = jnp.arange(experts * capacity, dtype=jnp.int32)
    hits = slot[:, :, None] == slot_ids[None, None, :]
    chosen = jnp.any(hits, axis=1).T.astype(jnp.bfloat16)
    outgoing = jnp.dot(chosen, normed, preferred_element_type=jnp.float32).astype(jnp.bfloat16)
    outgoing = outgoing.reshape(ep_count, local_experts, capacity, width)
    incoming = lax.all_to_all(outgoing, "ep", split_axis=0, concat_axis=0, tiled=True)
    gate_rows = jnp.einsum(
        "sjcd,jdf->sjcf", incoming, expert_gate, preferred_element_type=jnp.float32
    )
    up_rows = jnp.einsum("sjcd,jdf->sjcf", incoming, expert_up, preferred_element_type=jnp.float32)
    expert_hidden = (jax.nn.silu(gate_rows) * up_rows).astype(jnp.bfloat16)
    tp_index = lax.axis_index("tp")
    columns = width // tp_count
    down_blocks = expert_down.reshape(local_experts, -1, tp_count, columns).transpose(2, 0, 1, 3)
    own_block = lax.dynamic_index_in_dim(down_blocks, tp_index, 0, keepdims=False)
    expert_part = jnp.einsum(
        "sjcf,jfd->sjcd", expert_hidden, own_block, preferred_element_type=jnp.float32
    )
    for shift in range(1, tp_count):
        pairs = [(i, (i + shift) % tp_count) for i in range(tp_count)]
        wanted = lax.dynamic_index_in_dim(
            down_blocks, (tp_index + shift) % tp_count, 0, keepdims=False
        )
        peer_block = lax.ppermute(wanted, "tp", perm=pairs)
        peer_hidden = lax.ppermute(expert_hidden, "tp", perm=pairs)
        expert_part = expert_part + jnp.einsum(
            "sjcf,jfd->sjcd", peer_hidden, peer_block, preferred_element_type=jnp.float32
        )
    expert_cols = expert_part.astype(jnp.bfloat16)
    returned = lax.all_to_all(expert_cols, "ep", split_axis=0, concat_axis=0, tiled=True)
    flat_results = returned.reshape(experts * capacity, columns)
    mixing = jnp.sum(jnp.where(hits, route_weights[:, :, None], 0.0), axis=1)
    mixing_high = mixing.astype(jnp.bfloat16)
    mixing_low = (mixing - mixing_high.astype(jnp.float32)).astype(jnp.bfloat16)
    routed = jnp.dot(mixing_high, flat_results, preferred_element_type=jnp.float32) + jnp.dot(
        mixing_low, flat_results, preferred_element_type=jnp.float32
    )
    resid_cols = lax.dynamic_slice_in_dim(resid, lax.axis_index("tp") * columns, columns, 1)
    return (resid_cols + shared_scale[:, None] * shared_cols + routed).astype(jnp.bfloat16)


def solution(mesh):
    placed = (
        P("ep", None),
        P("ep", "tp"),
        P("ep", "tp"),
        P("ep", "tp"),
        P("ep", None),
        P("ep", None),
        P("ep", None),
        P("tp", None),
        P(),
        P("ep", None, "tp"),
        P("ep", None, "tp"),
        P("ep", "tp", None),
        P(None, "tp"),
        P(None, "tp"),
        P("tp", None),
        P(),
    )
    return jax.shard_map(
        on_device, mesh=mesh, in_specs=placed, out_specs=P("ep", "tp"), check_vma=False
    )
```

```python
import jax
import jax.numpy as jnp
from jax import lax
from jax.sharding import PartitionSpec as P

HEAD = 128


def slots_of(block_routes, experts, capacity):
    length, picks = block_routes.shape
    count = length * picks
    flat = block_routes.reshape(count)
    onehot = flat[:, None] == jnp.arange(experts, dtype=jnp.int32)[None, :]
    places = jnp.arange(count, dtype=jnp.int32)
    earlier = (places[:, None] > places[None, :]).astype(jnp.bfloat16)
    before = jnp.dot(earlier, onehot.astype(jnp.bfloat16), preferred_element_type=jnp.float32)
    rank = jnp.sum(jnp.where(onehot, before, 0.0), axis=1).astype(jnp.int32)
    slot = flat * capacity + rank
    return slot.reshape(length, picks)


def attend_local(query_block, key_block, value_block, segment):
    length = query_block.shape[0]
    heads = query_block.shape[1] // HEAD
    places = jnp.arange(length, dtype=jnp.int32)
    allowed = (segment[:, None] == segment[None, :]) & (places[:, None] >= places[None, :])
    query_heads = query_block.reshape(length, heads, HEAD)
    key_heads = key_block.reshape(length, heads, HEAD)
    value_heads = value_block.reshape(length, heads, HEAD)
    scores = jnp.einsum(
        "qhd,khd->hqk", query_heads, key_heads, preferred_element_type=jnp.float32
    ) * HEAD ** (-0.5)
    scores = jnp.where(allowed[None], scores, -jnp.inf)
    highest = jnp.max(scores, axis=2, keepdims=True)
    weights = jnp.exp(scores - highest)
    shares = (weights / jnp.sum(weights, axis=2, keepdims=True)).astype(jnp.bfloat16)
    attended = jnp.einsum("hqk,khd->qhd", shares, value_heads, preferred_element_type=jnp.float32)
    return attended.astype(jnp.bfloat16).reshape(length, heads * HEAD)


def on_device(
    stream,
    queries,
    keys_in,
    values_in,
    segment_ids,
    routes,
    route_weights,
    w_out,
    norm_gain,
    expert_gate,
    expert_up,
    expert_down,
    shared_gate,
    shared_up,
    shared_down,
    shared_router,
):
    length, width = stream.shape
    ep_count = lax.axis_size("ep")
    tp_count = lax.axis_size("tp")
    attended = attend_local(queries, keys_in, values_in, segment_ids[0])
    partial_value = jnp.dot(attended, w_out, preferred_element_type=jnp.float32)
    summed_cols = lax.psum_scatter(
        partial_value.astype(jnp.bfloat16), "tp", scatter_dimension=1, tiled=True
    )
    summed = lax.all_gather(summed_cols, "tp", axis=1, tiled=True)
    resid = stream.astype(jnp.float32) + summed.astype(jnp.float32)
    normed = (
        resid * lax.rsqrt(jnp.mean(resid * resid, axis=1, keepdims=True) + 1e-06) * norm_gain
    ).astype(jnp.bfloat16)
    shared_gate_rows = jnp.dot(normed, shared_gate, preferred_element_type=jnp.float32)
    shared_up_rows = jnp.dot(normed, shared_up, preferred_element_type=jnp.float32)
    shared_hidden = (jax.nn.silu(shared_gate_rows) * shared_up_rows).astype(jnp.bfloat16)
    shared_part = jnp.dot(shared_hidden, shared_down, preferred_element_type=jnp.float32)
    shared_cols = lax.psum_scatter(
        shared_part.astype(jnp.bfloat16), "tp", scatter_dimension=1, tiled=True
    ).astype(jnp.float32)
    shared_scale = jax.nn.sigmoid(
        jnp.dot(normed, shared_router, preferred_element_type=jnp.float32)
    )
    local_experts = expert_gate.shape[0]
    experts = local_experts * ep_count
    picks = routes.shape[1]
    divisor = 2 * experts * tp_count
    capacity = tp_count * ((3 * length * picks + divisor - 1) // divisor)
    slot = slots_of(routes, experts, capacity)
    slot_ids = jnp.arange(experts * capacity, dtype=jnp.int32)
    hits = slot[:, :, None] == slot_ids[None, None, :]
    chosen = jnp.any(hits, axis=1).T.astype(jnp.bfloat16)
    outgoing = jnp.dot(chosen, normed, preferred_element_type=jnp.float32).astype(jnp.bfloat16)
    outgoing = outgoing.reshape(ep_count, local_experts, capacity, width)
    incoming = lax.all_to_all(outgoing, "ep", split_axis=0, concat_axis=0, tiled=True)
    gate_rows = jnp.einsum(
        "sjcd,jdf->sjcf", incoming, expert_gate, preferred_element_type=jnp.float32
    )
    up_rows = jnp.einsum("sjcd,jdf->sjcf", incoming, expert_up, preferred_element_type=jnp.float32)
    expert_hidden = (jax.nn.silu(gate_rows) * up_rows).astype(jnp.bfloat16)
    expert_part = jnp.einsum(
        "sjcf,jfd->sjcd", expert_hidden, expert_down, preferred_element_type=jnp.float32
    )
    expert_cols = lax.psum_scatter(
        expert_part.astype(jnp.bfloat16), "tp", scatter_dimension=3, tiled=True
    )
    returned = lax.all_to_all(expert_cols, "ep", split_axis=0, concat_axis=0, tiled=True)
    columns = returned.shape[3]
    flat_results = returned.reshape(experts * capacity, columns)
    mixing = jnp.sum(jnp.where(hits, route_weights[:, :, None], 0.0), axis=1)
    mixing_high = mixing.astype(jnp.bfloat16)
    mixing_low = (mixing - mixing_high.astype(jnp.float32)).astype(jnp.bfloat16)
    routed = jnp.dot(mixing_high, flat_results, preferred_element_type=jnp.float32) + jnp.dot(
        mixing_low, flat_results, preferred_element_type=jnp.float32
    )
    resid_cols = lax.dynamic_slice_in_dim(resid, lax.axis_index("tp") * columns, columns, 1)
    return (resid_cols + shared_scale[:, None] * shared_cols + routed).astype(jnp.bfloat16)


def solution(mesh):
    placed = (
        P("ep", None),
        P("ep", "tp"),
        P("ep", "tp"),
        P("ep", "tp"),
        P("ep", None),
        P("ep", None),
        P("ep", None),
        P("tp", None),
        P(),
        P("ep", None, "tp"),
        P("ep", None, "tp"),
        P("ep", "tp", None),
        P(None, "tp"),
        P(None, "tp"),
        P("tp", None),
        P(),
    )
    return jax.shard_map(
        on_device, mesh=mesh, in_specs=placed, out_specs=P("ep", "tp"), check_vma=False
    )
```

```python
import jax
import jax.numpy as jnp
from jax import lax
from jax.sharding import PartitionSpec as P

HEAD = 128


def slots_of(block_routes, experts, capacity):
    length, picks = block_routes.shape
    count = length * picks
    flat = block_routes.reshape(count)
    onehot = flat[:, None] == jnp.arange(experts, dtype=jnp.int32)[None, :]
    places = jnp.arange(count, dtype=jnp.int32)
    earlier = (places[:, None] > places[None, :]).astype(jnp.bfloat16)
    before = jnp.dot(earlier, onehot.astype(jnp.bfloat16), preferred_element_type=jnp.float32)
    rank = jnp.sum(jnp.where(onehot, before, 0.0), axis=1).astype(jnp.int32)
    slot = flat * capacity + rank
    return slot.reshape(length, picks)


def attend_local(query_block, key_block, value_block, segment):
    length = query_block.shape[0]
    heads = query_block.shape[1] // HEAD
    places = jnp.arange(length, dtype=jnp.int32)
    allowed = (segment[:, None] == segment[None, :]) & (places[:, None] >= places[None, :])
    query_heads = query_block.reshape(length, heads, HEAD)
    key_heads = key_block.reshape(length, heads, HEAD)
    value_heads = value_block.reshape(length, heads, HEAD)
    scores = jnp.einsum(
        "qhd,khd->hqk", query_heads, key_heads, preferred_element_type=jnp.float32
    ) * HEAD ** (-0.5)
    scores = jnp.where(allowed[None], scores, -jnp.inf)
    highest = jnp.max(scores, axis=2, keepdims=True)
    weights = jnp.exp(scores - highest)
    shares = (weights / jnp.sum(weights, axis=2, keepdims=True)).astype(jnp.bfloat16)
    attended = jnp.einsum("hqk,khd->qhd", shares, value_heads, preferred_element_type=jnp.float32)
    return attended.astype(jnp.bfloat16).reshape(length, heads * HEAD)


def on_device(
    stream,
    queries,
    keys_in,
    values_in,
    segment_ids,
    routes,
    route_weights,
    w_out,
    norm_gain,
    expert_gate,
    expert_up,
    expert_down,
    shared_gate,
    shared_up,
    shared_down,
    shared_router,
):
    length, width = stream.shape
    ep_count = lax.axis_size("ep")
    tp_count = lax.axis_size("tp")
    attended = attend_local(queries, keys_in, values_in, segment_ids[0])
    partial_value = jnp.dot(attended, w_out, preferred_element_type=jnp.float32)
    summed_cols = lax.psum_scatter(
        partial_value.astype(jnp.bfloat16), "tp", scatter_dimension=1, tiled=True
    )
    summed = lax.all_gather(summed_cols, "tp", axis=1, tiled=True)
    resid = stream.astype(jnp.float32) + summed.astype(jnp.float32)
    normed = (
        resid * lax.rsqrt(jnp.mean(resid * resid, axis=1, keepdims=True) + 1e-06) * norm_gain
    ).astype(jnp.bfloat16)
    shared_gate_rows = jnp.dot(normed, shared_gate, preferred_element_type=jnp.float32)
    shared_up_rows = jnp.dot(normed, shared_up, preferred_element_type=jnp.float32)
    shared_hidden = (jax.nn.silu(shared_gate_rows) * shared_up_rows).astype(jnp.bfloat16)
    shared_part = jnp.dot(shared_hidden, shared_down, preferred_element_type=jnp.float32)
    shared_cols = lax.psum_scatter(
        shared_part.astype(jnp.bfloat16), "tp", scatter_dimension=1, tiled=True
    ).astype(jnp.float32)
    shared_scale = jax.nn.sigmoid(
        jnp.dot(normed, shared_router, preferred_element_type=jnp.float32)
    )
    local_experts = expert_gate.shape[0]
    experts = local_experts * ep_count
    picks = routes.shape[1]
    divisor = 2 * experts * tp_count
    capacity = tp_count * ((3 * length * picks + divisor - 1) // divisor)
    slot = slots_of(routes, experts, capacity)
    slot_ids = jnp.arange(experts * capacity, dtype=jnp.int32)
    hits = slot[:, :, None] == slot_ids[None, None, :]
    chosen = jnp.any(hits, axis=1).T.astype(jnp.bfloat16)
    outgoing = jnp.dot(chosen, normed, preferred_element_type=jnp.float32).astype(jnp.bfloat16)
    outgoing = outgoing.reshape(ep_count, local_experts, capacity, width)
    incoming = lax.all_to_all(outgoing, "ep", split_axis=0, concat_axis=0, tiled=True)
    gate_rows = jnp.einsum(
        "sjcd,jdf->sjcf", incoming, expert_gate, preferred_element_type=jnp.float32
    )
    up_rows = jnp.einsum("sjcd,jdf->sjcf", incoming, expert_up, preferred_element_type=jnp.float32)
    expert_hidden = (jax.nn.silu(gate_rows) * up_rows).astype(jnp.bfloat16)
    expert_part = jnp.einsum(
        "sjcf,jfd->sjcd", expert_hidden, expert_down, preferred_element_type=jnp.float32
    )
    expert_cols = lax.psum_scatter(
        expert_part.astype(jnp.bfloat16), "tp", scatter_dimension=3, tiled=True
    )
    returned = lax.all_to_all(expert_cols, "ep", split_axis=0, concat_axis=0, tiled=True)
    columns = returned.shape[3]
    flat_results = returned.reshape(experts * capacity, columns)
    mixing = jnp.sum(jnp.where(hits, route_weights[:, :, None], 0.0), axis=1)
    mixing_high = mixing.astype(jnp.bfloat16)
    mixing_low = (mixing - mixing_high.astype(jnp.float32)).astype(jnp.bfloat16)
    mixing_high, mixing_low = lax.optimization_barrier((mixing_high, mixing_low))
    routed = jnp.dot(mixing_high, flat_results, preferred_element_type=jnp.float32) + jnp.dot(
        mixing_low, flat_results, preferred_element_type=jnp.float32
    )
    resid_cols = lax.dynamic_slice_in_dim(resid, lax.axis_index("tp") * columns, columns, 1)
    return (resid_cols + shared_scale[:, None] * shared_cols + routed).astype(jnp.bfloat16)


def solution(mesh):
    placed = (
        P("ep", None),
        P("ep", "tp"),
        P("ep", "tp"),
        P("ep", "tp"),
        P("ep", None),
        P("ep", None),
        P("ep", None),
        P("tp", None),
        P(),
        P("ep", None, "tp"),
        P("ep", None, "tp"),
        P("ep", "tp", None),
        P(None, "tp"),
        P(None, "tp"),
        P("tp", None),
        P(),
    )
    return jax.shard_map(
        on_device, mesh=mesh, in_specs=placed, out_specs=P("ep", "tp"), check_vma=False
    )
```

```python
import jax
import jax.numpy as jnp
from jax import lax
from jax.sharding import PartitionSpec as P

HEAD = 128


def slots_of(block_routes, experts, capacity):
    length, picks = block_routes.shape
    count = length * picks
    flat = block_routes.reshape(count)
    onehot = flat[:, None] == jnp.arange(experts, dtype=jnp.int32)[None, :]
    places = jnp.arange(count, dtype=jnp.int32)
    earlier = (places[:, None] > places[None, :]).astype(jnp.bfloat16)
    before = jnp.dot(earlier, onehot.astype(jnp.bfloat16), preferred_element_type=jnp.float32)
    rank = jnp.sum(jnp.where(onehot, before, 0.0), axis=1).astype(jnp.int32)
    slot = flat * capacity + rank
    return slot.reshape(length, picks)


def attend_local(query_block, key_block, value_block, segment):
    length = query_block.shape[0]
    heads = query_block.shape[1] // HEAD
    places = jnp.arange(length, dtype=jnp.int32)
    allowed = (segment[:, None] == segment[None, :]) & (places[:, None] >= places[None, :])
    query_heads = query_block.reshape(length, heads, HEAD)
    key_heads = key_block.reshape(length, heads, HEAD)
    value_heads = value_block.reshape(length, heads, HEAD)
    scores = jnp.einsum(
        "qhd,khd->hqk", query_heads, key_heads, preferred_element_type=jnp.float32
    ) * HEAD ** (-0.5)
    scores = jnp.where(allowed[None], scores, -jnp.inf)
    highest = jnp.max(scores, axis=2, keepdims=True)
    weights = jnp.exp(scores - highest)
    shares = (weights / jnp.sum(weights, axis=2, keepdims=True)).astype(jnp.bfloat16)
    attended = jnp.einsum("hqk,khd->qhd", shares, value_heads, preferred_element_type=jnp.float32)
    return attended.astype(jnp.bfloat16).reshape(length, heads * HEAD)


def on_device(
    stream,
    queries,
    keys_in,
    values_in,
    segment_ids,
    routes,
    route_weights,
    w_out,
    norm_gain,
    expert_gate,
    expert_up,
    expert_down,
    shared_gate,
    shared_up,
    shared_down,
    shared_router,
):
    length, width = stream.shape
    ep_count = lax.axis_size("ep")
    tp_count = lax.axis_size("tp")
    attended = attend_local(queries, keys_in, values_in, segment_ids[0])
    partial_value = jnp.dot(attended, w_out, preferred_element_type=jnp.float32)
    summed_cols = lax.psum_scatter(
        partial_value.astype(jnp.bfloat16), "tp", scatter_dimension=1, tiled=True
    )
    summed = lax.all_gather(summed_cols, "tp", axis=1, tiled=True)
    resid = stream.astype(jnp.float32) + summed.astype(jnp.float32)
    normed = (
        resid * lax.rsqrt(jnp.mean(resid * resid, axis=1, keepdims=True) + 1e-06) * norm_gain
    ).astype(jnp.bfloat16)
    shared_gate_rows = jnp.dot(normed, shared_gate, preferred_element_type=jnp.float32)
    shared_up_rows = jnp.dot(normed, shared_up, preferred_element_type=jnp.float32)
    shared_hidden = (jax.nn.silu(shared_gate_rows) * shared_up_rows).astype(jnp.bfloat16)
    shared_part = jnp.dot(shared_hidden, shared_down, preferred_element_type=jnp.float32)
    shared_cols = lax.psum_scatter(
        shared_part.astype(jnp.bfloat16), "tp", scatter_dimension=1, tiled=True
    ).astype(jnp.float32)
    shared_scale = jax.nn.sigmoid(
        jnp.dot(normed, shared_router, preferred_element_type=jnp.float32)
    )
    local_experts = expert_gate.shape[0]
    experts = local_experts * ep_count
    picks = routes.shape[1]
    divisor = 2 * experts * tp_count
    capacity = tp_count * ((3 * length * picks + divisor - 1) // divisor)
    slot = slots_of(routes, experts, capacity)
    slot_ids = jnp.arange(experts * capacity, dtype=jnp.int32)
    hits = slot[:, :, None] == slot_ids[None, None, :]
    chosen = jnp.any(hits, axis=1).T.astype(jnp.bfloat16)
    outgoing = jnp.dot(chosen, normed, preferred_element_type=jnp.float32).astype(jnp.bfloat16)
    outgoing = outgoing.reshape(ep_count, local_experts, capacity, width)
    incoming = lax.all_to_all(outgoing, "ep", split_axis=0, concat_axis=0, tiled=True)
    gate_rows = jnp.einsum(
        "sjcd,jdf->sjcf", incoming, expert_gate, preferred_element_type=jnp.float32
    )
    up_rows = jnp.einsum("sjcd,jdf->sjcf", incoming, expert_up, preferred_element_type=jnp.float32)
    expert_hidden = (jax.nn.silu(gate_rows) * up_rows).astype(jnp.bfloat16)
    mixing = jnp.sum(jnp.where(hits, route_weights[:, :, None], 0.0), axis=1)
    mixing_high = mixing.astype(jnp.bfloat16)
    mixing_low = (mixing - mixing_high.astype(jnp.float32)).astype(jnp.bfloat16)
    mixing_high, mixing_low = lax.optimization_barrier((mixing_high, mixing_low))
    mixing_high = mixing_high.reshape(length, ep_count, local_experts, capacity)
    mixing_low = mixing_low.reshape(length, ep_count, local_experts, capacity)
    routed = None
    for index in range(local_experts):
        expert_part = jnp.einsum(
            "scf,fd->scd",
            expert_hidden[:, index],
            expert_down[index],
            preferred_element_type=jnp.float32,
        )
        expert_cols = lax.psum_scatter(
            expert_part.astype(jnp.bfloat16), "tp", scatter_dimension=2, tiled=True
        )
        returned = lax.all_to_all(expert_cols, "ep", split_axis=0, concat_axis=0, tiled=True)
        columns = returned.shape[2]
        flat_results = returned.reshape(ep_count * capacity, columns)
        high = mixing_high[:, :, index].reshape(length, ep_count * capacity)
        low = mixing_low[:, :, index].reshape(length, ep_count * capacity)
        term = jnp.dot(high, flat_results, preferred_element_type=jnp.float32) + jnp.dot(
            low, flat_results, preferred_element_type=jnp.float32
        )
        routed = term if routed is None else routed + term
    resid_cols = lax.dynamic_slice_in_dim(resid, lax.axis_index("tp") * columns, columns, 1)
    return (resid_cols + shared_scale[:, None] * shared_cols + routed).astype(jnp.bfloat16)


def solution(mesh):
    placed = (
        P("ep", None),
        P("ep", "tp"),
        P("ep", "tp"),
        P("ep", "tp"),
        P("ep", None),
        P("ep", None),
        P("ep", None),
        P("tp", None),
        P(),
        P("ep", None, "tp"),
        P("ep", None, "tp"),
        P("ep", "tp", None),
        P(None, "tp"),
        P(None, "tp"),
        P("tp", None),
        P(),
    )
    return jax.shard_map(
        on_device, mesh=mesh, in_specs=placed, out_specs=P("ep", "tp"), check_vma=False
    )
```

```python
import jax
import jax.numpy as jnp
from jax import lax
from jax.sharding import PartitionSpec as P

HEAD = 128


def slots_of(block_routes, experts, capacity):
    length, picks = block_routes.shape
    count = length * picks
    flat = block_routes.reshape(count)
    onehot = flat[:, None] == jnp.arange(experts, dtype=jnp.int32)[None, :]
    places = jnp.arange(count, dtype=jnp.int32)
    earlier = (places[:, None] > places[None, :]).astype(jnp.bfloat16)
    before = jnp.dot(earlier, onehot.astype(jnp.bfloat16), preferred_element_type=jnp.float32)
    rank = jnp.sum(jnp.where(onehot, before, 0.0), axis=1).astype(jnp.int32)
    slot = flat * capacity + rank
    return slot.reshape(length, picks)


def attend_local(query_block, key_block, value_block, segment):
    length = query_block.shape[0]
    heads = query_block.shape[1] // HEAD
    places = jnp.arange(length, dtype=jnp.int32)
    allowed = (segment[:, None] == segment[None, :]) & (places[:, None] >= places[None, :])
    query_heads = query_block.reshape(length, heads, HEAD)
    key_heads = key_block.reshape(length, heads, HEAD)
    value_heads = value_block.reshape(length, heads, HEAD)
    scores = jnp.einsum(
        "qhd,khd->hqk", query_heads, key_heads, preferred_element_type=jnp.float32
    ) * HEAD ** (-0.5)
    scores = jnp.where(allowed[None], scores, -jnp.inf)
    highest = jnp.max(scores, axis=2, keepdims=True)
    weights = jnp.exp(scores - highest)
    shares = (weights / jnp.sum(weights, axis=2, keepdims=True)).astype(jnp.bfloat16)
    attended = jnp.einsum("hqk,khd->qhd", shares, value_heads, preferred_element_type=jnp.float32)
    return attended.astype(jnp.bfloat16).reshape(length, heads * HEAD)


def on_device(
    stream,
    queries,
    keys_in,
    values_in,
    segment_ids,
    routes,
    route_weights,
    w_out,
    norm_gain,
    expert_gate,
    expert_up,
    expert_down,
    shared_gate,
    shared_up,
    shared_down,
    shared_router,
):
    length, width = stream.shape
    ep_count = lax.axis_size("ep")
    tp_count = lax.axis_size("tp")
    attended = attend_local(queries, keys_in, values_in, segment_ids[0])
    partial_value = jnp.dot(attended, w_out, preferred_element_type=jnp.float32)
    summed_cols = lax.psum_scatter(
        partial_value.astype(jnp.bfloat16), "tp", scatter_dimension=1, tiled=True
    )
    summed = lax.all_gather(summed_cols, "tp", axis=1, tiled=True)
    resid = stream.astype(jnp.float32) + summed.astype(jnp.float32)
    normed = (
        resid * lax.rsqrt(jnp.mean(resid * resid, axis=1, keepdims=True) + 1e-06) * norm_gain
    ).astype(jnp.bfloat16)
    shared_gate_rows = jnp.dot(normed, shared_gate, preferred_element_type=jnp.float32)
    shared_up_rows = jnp.dot(normed, shared_up, preferred_element_type=jnp.float32)
    shared_hidden = (jax.nn.silu(shared_gate_rows) * shared_up_rows).astype(jnp.bfloat16)
    shared_part = jnp.dot(shared_hidden, shared_down, preferred_element_type=jnp.float32)
    shared_cols = lax.psum_scatter(
        shared_part.astype(jnp.bfloat16), "tp", scatter_dimension=1, tiled=True
    ).astype(jnp.float32)
    shared_scale = jax.nn.sigmoid(
        jnp.dot(normed, shared_router, preferred_element_type=jnp.float32)
    )
    local_experts = expert_gate.shape[0]
    experts = local_experts * ep_count
    picks = routes.shape[1]
    divisor = 2 * experts * tp_count
    capacity = tp_count * ((3 * length * picks + divisor - 1) // divisor)
    slot = slots_of(routes, experts, capacity)
    slot_ids = jnp.arange(experts * capacity, dtype=jnp.int32)
    hits = slot[:, :, None] == slot_ids[None, None, :]
    chosen = jnp.any(hits, axis=1).T.astype(jnp.bfloat16)
    outgoing = jnp.dot(chosen, normed, preferred_element_type=jnp.float32).astype(jnp.bfloat16)
    outgoing = outgoing.reshape(ep_count, local_experts, capacity, width)
    incoming = lax.all_to_all(outgoing, "ep", split_axis=0, concat_axis=0, tiled=True)
    gate_rows = jnp.einsum(
        "sjcd,jdf->sjcf", incoming, expert_gate, preferred_element_type=jnp.float32
    )
    up_rows = jnp.einsum("sjcd,jdf->sjcf", incoming, expert_up, preferred_element_type=jnp.float32)
    expert_hidden = (jax.nn.silu(gate_rows) * up_rows).astype(jnp.bfloat16)
    slot_grid = (
        jnp.arange(ep_count, dtype=jnp.int32)[:, None, None] * local_experts
        + jnp.arange(local_experts, dtype=jnp.int32)[None, :, None]
    ) * capacity + jnp.arange(capacity, dtype=jnp.int32)[None, None, :]
    mixes = []
    for index in range(local_experts):
        ids = slot_grid[:, index].reshape(-1)
        hit = slot[:, :, None] == ids[None, None, :]
        mixing = jnp.sum(jnp.where(hit, route_weights[:, :, None], 0.0), axis=1)
        high = mixing.astype(jnp.bfloat16)
        low = (mixing - high.astype(jnp.float32)).astype(jnp.bfloat16)
        mixes.append((high, low))
    routed = None
    for index in range(local_experts):
        expert_part = jnp.einsum(
            "scf,fd->scd",
            expert_hidden[:, index],
            expert_down[index],
            preferred_element_type=jnp.float32,
        ).astype(jnp.bfloat16)
        if index == local_experts - 1:
            expert_part, mixes = lax.optimization_barrier((expert_part, mixes))
        expert_cols = lax.psum_scatter(expert_part, "tp", scatter_dimension=2, tiled=True)
        returned = lax.all_to_all(expert_cols, "ep", split_axis=0, concat_axis=0, tiled=True)
        columns = returned.shape[2]
        flat_results = returned.reshape(ep_count * capacity, columns)
        high, low = mixes[index]
        term = jnp.dot(high, flat_results, preferred_element_type=jnp.float32) + jnp.dot(
            low, flat_results, preferred_element_type=jnp.float32
        )
        routed = term if routed is None else routed + term
    resid_cols = lax.dynamic_slice_in_dim(resid, lax.axis_index("tp") * columns, columns, 1)
    return (resid_cols + shared_scale[:, None] * shared_cols + routed).astype(jnp.bfloat16)


def solution(mesh):
    placed = (
        P("ep", None),
        P("ep", "tp"),
        P("ep", "tp"),
        P("ep", "tp"),
        P("ep", None),
        P("ep", None),
        P("ep", None),
        P("tp", None),
        P(),
        P("ep", None, "tp"),
        P("ep", None, "tp"),
        P("ep", "tp", None),
        P(None, "tp"),
        P(None, "tp"),
        P("tp", None),
        P(),
    )
    return jax.shard_map(
        on_device, mesh=mesh, in_specs=placed, out_specs=P("ep", "tp"), check_vma=False
    )
```

```python
import jax
import jax.numpy as jnp
from jax import lax
from jax.sharding import PartitionSpec as P

HEAD = 128


def slots_of(block_routes, experts, capacity):
    length, picks = block_routes.shape
    count = length * picks
    flat = block_routes.reshape(count)
    onehot = flat[:, None] == jnp.arange(experts, dtype=jnp.int32)[None, :]
    places = jnp.arange(count, dtype=jnp.int32)
    earlier = (places[:, None] > places[None, :]).astype(jnp.bfloat16)
    before = jnp.dot(earlier, onehot.astype(jnp.bfloat16), preferred_element_type=jnp.float32)
    rank = jnp.sum(jnp.where(onehot, before, 0.0), axis=1).astype(jnp.int32)
    slot = flat * capacity + rank
    return slot.reshape(length, picks)


def attend_local(query_block, key_block, value_block, segment):
    length = query_block.shape[0]
    heads = query_block.shape[1] // HEAD
    places = jnp.arange(length, dtype=jnp.int32)
    allowed = (segment[:, None] == segment[None, :]) & (places[:, None] >= places[None, :])
    query_heads = query_block.reshape(length, heads, HEAD)
    key_heads = key_block.reshape(length, heads, HEAD)
    value_heads = value_block.reshape(length, heads, HEAD)
    scores = jnp.einsum(
        "qhd,khd->hqk", query_heads, key_heads, preferred_element_type=jnp.float32
    ) * HEAD ** (-0.5)
    scores = jnp.where(allowed[None], scores, -jnp.inf)
    highest = jnp.max(scores, axis=2, keepdims=True)
    weights = jnp.exp(scores - highest)
    shares = (weights / jnp.sum(weights, axis=2, keepdims=True)).astype(jnp.bfloat16)
    attended = jnp.einsum("hqk,khd->qhd", shares, value_heads, preferred_element_type=jnp.float32)
    return attended.astype(jnp.bfloat16).reshape(length, heads * HEAD)


def on_device(
    stream,
    queries,
    keys_in,
    values_in,
    segment_ids,
    routes,
    route_weights,
    w_out,
    norm_gain,
    expert_gate,
    expert_up,
    expert_down,
    shared_gate,
    shared_up,
    shared_down,
    shared_router,
):
    length, width = stream.shape
    ep_count = lax.axis_size("ep")
    tp_count = lax.axis_size("tp")
    attended = attend_local(queries, keys_in, values_in, segment_ids[0])
    partial_value = jnp.dot(attended, w_out, preferred_element_type=jnp.float32)
    summed_cols = lax.psum_scatter(
        partial_value.astype(jnp.bfloat16), "tp", scatter_dimension=1, tiled=True
    )
    summed = lax.all_gather(summed_cols, "tp", axis=1, tiled=True)
    resid = stream.astype(jnp.float32) + summed.astype(jnp.float32)
    normed = (
        resid * lax.rsqrt(jnp.mean(resid * resid, axis=1, keepdims=True) + 1e-06) * norm_gain
    ).astype(jnp.bfloat16)
    shared_gate_rows = jnp.dot(normed, shared_gate, preferred_element_type=jnp.float32)
    shared_up_rows = jnp.dot(normed, shared_up, preferred_element_type=jnp.float32)
    shared_hidden = (jax.nn.silu(shared_gate_rows) * shared_up_rows).astype(jnp.bfloat16)
    shared_part = jnp.dot(shared_hidden, shared_down, preferred_element_type=jnp.float32)
    shared_cols = lax.psum_scatter(
        shared_part.astype(jnp.bfloat16), "tp", scatter_dimension=1, tiled=True
    ).astype(jnp.float32)
    shared_scale = jax.nn.sigmoid(
        jnp.dot(normed, shared_router, preferred_element_type=jnp.float32)
    )
    local_experts = expert_gate.shape[0]
    experts = local_experts * ep_count
    picks = routes.shape[1]
    divisor = 2 * experts * tp_count
    capacity = tp_count * ((3 * length * picks + divisor - 1) // divisor)
    slot = slots_of(routes, experts, capacity)
    slot_ids = jnp.arange(experts * capacity, dtype=jnp.int32)
    hits = slot[:, :, None] == slot_ids[None, None, :]
    chosen = jnp.any(hits, axis=1).T.astype(jnp.bfloat16)
    outgoing = jnp.dot(chosen, normed, preferred_element_type=jnp.float32).astype(jnp.bfloat16)
    outgoing = outgoing.reshape(ep_count, local_experts, capacity, width)
    incoming = lax.all_to_all(outgoing, "ep", split_axis=0, concat_axis=0, tiled=True)
    slot_grid = (
        jnp.arange(ep_count, dtype=jnp.int32)[:, None, None] * local_experts
        + jnp.arange(local_experts, dtype=jnp.int32)[None, :, None]
    ) * capacity + jnp.arange(capacity, dtype=jnp.int32)[None, None, :]
    mixes = []
    for index in range(local_experts):
        ids = slot_grid[:, index].reshape(-1)
        hit = slot[:, :, None] == ids[None, None, :]
        mixing = jnp.sum(jnp.where(hit, route_weights[:, :, None], 0.0), axis=1)
        high = mixing.astype(jnp.bfloat16)
        low = (mixing - high.astype(jnp.float32)).astype(jnp.bfloat16)
        mixes.append((high, low))
    routed = None
    for index in range(local_experts):
        rows = incoming[:, index]
        gate_rows = jnp.einsum(
            "scd,df->scf", rows, expert_gate[index], preferred_element_type=jnp.float32
        )
        up_rows = jnp.einsum(
            "scd,df->scf", rows, expert_up[index], preferred_element_type=jnp.float32
        )
        expert_hidden = (jax.nn.silu(gate_rows) * up_rows).astype(jnp.bfloat16)
        expert_part = jnp.einsum(
            "scf,fd->scd",
            expert_hidden,
            expert_down[index],
            preferred_element_type=jnp.float32,
        ).astype(jnp.bfloat16)
        if index == local_experts - 1:
            expert_part, mixes = lax.optimization_barrier((expert_part, mixes))
        expert_cols = lax.psum_scatter(expert_part, "tp", scatter_dimension=2, tiled=True)
        returned = lax.all_to_all(expert_cols, "ep", split_axis=0, concat_axis=0, tiled=True)
        columns = returned.shape[2]
        flat_results = returned.reshape(ep_count * capacity, columns)
        high, low = mixes[index]
        term = jnp.dot(high, flat_results, preferred_element_type=jnp.float32) + jnp.dot(
            low, flat_results, preferred_element_type=jnp.float32
        )
        routed = term if routed is None else routed + term
    resid_cols = lax.dynamic_slice_in_dim(resid, lax.axis_index("tp") * columns, columns, 1)
    return (resid_cols + shared_scale[:, None] * shared_cols + routed).astype(jnp.bfloat16)


def solution(mesh):
    placed = (
        P("ep", None),
        P("ep", "tp"),
        P("ep", "tp"),
        P("ep", "tp"),
        P("ep", None),
        P("ep", None),
        P("ep", None),
        P("tp", None),
        P(),
        P("ep", None, "tp"),
        P("ep", None, "tp"),
        P("ep", "tp", None),
        P(None, "tp"),
        P(None, "tp"),
        P("tp", None),
        P(),
    )
    return jax.shard_map(
        on_device, mesh=mesh, in_specs=placed, out_specs=P("ep", "tp"), check_vma=False
    )
```

```python
import jax
import jax.numpy as jnp
from jax import lax
from jax.sharding import PartitionSpec as P

HEAD = 128


def slots_of(block_routes, experts, capacity):
    length, picks = block_routes.shape
    count = length * picks
    flat = block_routes.reshape(count)
    onehot = flat[:, None] == jnp.arange(experts, dtype=jnp.int32)[None, :]
    places = jnp.arange(count, dtype=jnp.int32)
    earlier = (places[:, None] > places[None, :]).astype(jnp.bfloat16)
    before = jnp.dot(earlier, onehot.astype(jnp.bfloat16), preferred_element_type=jnp.float32)
    rank = jnp.sum(jnp.where(onehot, before, 0.0), axis=1).astype(jnp.int32)
    slot = flat * capacity + rank
    return slot.reshape(length, picks)


def attend_local(query_block, key_block, value_block, segment):
    length = query_block.shape[0]
    heads = query_block.shape[1] // HEAD
    places = jnp.arange(length, dtype=jnp.int32)
    allowed = (segment[:, None] == segment[None, :]) & (places[:, None] >= places[None, :])
    query_heads = query_block.reshape(length, heads, HEAD)
    key_heads = key_block.reshape(length, heads, HEAD)
    value_heads = value_block.reshape(length, heads, HEAD)
    scores = jnp.einsum(
        "qhd,khd->hqk", query_heads, key_heads, preferred_element_type=jnp.float32
    ) * HEAD ** (-0.5)
    scores = jnp.where(allowed[None], scores, -jnp.inf)
    highest = jnp.max(scores, axis=2, keepdims=True)
    weights = jnp.exp(scores - highest)
    shares = (weights / jnp.sum(weights, axis=2, keepdims=True)).astype(jnp.bfloat16)
    attended = jnp.einsum("hqk,khd->qhd", shares, value_heads, preferred_element_type=jnp.float32)
    return attended.astype(jnp.bfloat16).reshape(length, heads * HEAD)


def on_device(
    stream,
    queries,
    keys_in,
    values_in,
    segment_ids,
    routes,
    route_weights,
    w_out,
    norm_gain,
    expert_gate,
    expert_up,
    expert_down,
    shared_gate,
    shared_up,
    shared_down,
    shared_router,
):
    length, width = stream.shape
    ep_count = lax.axis_size("ep")
    tp_count = lax.axis_size("tp")
    attended = attend_local(queries, keys_in, values_in, segment_ids[0])
    partial_value = jnp.dot(attended, w_out, preferred_element_type=jnp.float32)
    summed_cols = lax.psum_scatter(
        partial_value.astype(jnp.bfloat16), "tp", scatter_dimension=1, tiled=True
    )
    summed = lax.all_gather(summed_cols, "tp", axis=1, tiled=True)
    resid = stream.astype(jnp.float32) + summed.astype(jnp.float32)
    normed = (
        resid * lax.rsqrt(jnp.mean(resid * resid, axis=1, keepdims=True) + 1e-06) * norm_gain
    ).astype(jnp.bfloat16)
    shared_gate_rows = jnp.dot(normed, shared_gate, preferred_element_type=jnp.float32)
    shared_up_rows = jnp.dot(normed, shared_up, preferred_element_type=jnp.float32)
    shared_hidden = (jax.nn.silu(shared_gate_rows) * shared_up_rows).astype(jnp.bfloat16)
    shared_part = jnp.dot(shared_hidden, shared_down, preferred_element_type=jnp.float32)
    shared_cols = lax.psum_scatter(
        shared_part.astype(jnp.bfloat16), "tp", scatter_dimension=1, tiled=True
    ).astype(jnp.float32)
    shared_scale = jax.nn.sigmoid(
        jnp.dot(normed, shared_router, preferred_element_type=jnp.float32)
    )
    local_experts = expert_gate.shape[0]
    experts = local_experts * ep_count
    picks = routes.shape[1]
    divisor = 2 * experts * tp_count
    capacity = tp_count * ((3 * length * picks + divisor - 1) // divisor)
    slot = slots_of(routes, experts, capacity)
    slot_ids = jnp.arange(experts * capacity, dtype=jnp.int32)
    hits = slot[:, :, None] == slot_ids[None, None, :]
    chosen = jnp.any(hits, axis=1).T.astype(jnp.bfloat16)
    chosen = chosen.reshape(ep_count, local_experts, capacity, length)
    slot_grid = (
        jnp.arange(ep_count, dtype=jnp.int32)[:, None, None] * local_experts
        + jnp.arange(local_experts, dtype=jnp.int32)[None, :, None]
    ) * capacity + jnp.arange(capacity, dtype=jnp.int32)[None, None, :]
    mixes = []
    for index in range(local_experts):
        ids = slot_grid[:, index].reshape(-1)
        hit = slot[:, :, None] == ids[None, None, :]
        mixing = jnp.sum(jnp.where(hit, route_weights[:, :, None], 0.0), axis=1)
        high = mixing.astype(jnp.bfloat16)
        low = (mixing - high.astype(jnp.float32)).astype(jnp.bfloat16)
        mixes.append((high, low))
    routed = None
    for index in range(local_experts):
        outgoing = jnp.einsum(
            "sct,td->scd", chosen[:, index], normed, preferred_element_type=jnp.float32
        ).astype(jnp.bfloat16)
        rows = lax.all_to_all(outgoing, "ep", split_axis=0, concat_axis=0, tiled=True)
        gate_rows = jnp.einsum(
            "scd,df->scf", rows, expert_gate[index], preferred_element_type=jnp.float32
        )
        up_rows = jnp.einsum(
            "scd,df->scf", rows, expert_up[index], preferred_element_type=jnp.float32
        )
        expert_hidden = (jax.nn.silu(gate_rows) * up_rows).astype(jnp.bfloat16)
        expert_part = jnp.einsum(
            "scf,fd->scd",
            expert_hidden,
            expert_down[index],
            preferred_element_type=jnp.float32,
        ).astype(jnp.bfloat16)
        if index == local_experts - 1:
            expert_part, mixes = lax.optimization_barrier((expert_part, mixes))
        expert_cols = lax.psum_scatter(expert_part, "tp", scatter_dimension=2, tiled=True)
        returned = lax.all_to_all(expert_cols, "ep", split_axis=0, concat_axis=0, tiled=True)
        columns = returned.shape[2]
        flat_results = returned.reshape(ep_count * capacity, columns)
        high, low = mixes[index]
        term = jnp.dot(high, flat_results, preferred_element_type=jnp.float32) + jnp.dot(
            low, flat_results, preferred_element_type=jnp.float32
        )
        routed = term if routed is None else routed + term
    resid_cols = lax.dynamic_slice_in_dim(resid, lax.axis_index("tp") * columns, columns, 1)
    return (resid_cols + shared_scale[:, None] * shared_cols + routed).astype(jnp.bfloat16)


def solution(mesh):
    placed = (
        P("ep", None),
        P("ep", "tp"),
        P("ep", "tp"),
        P("ep", "tp"),
        P("ep", None),
        P("ep", None),
        P("ep", None),
        P("tp", None),
        P(),
        P("ep", None, "tp"),
        P("ep", None, "tp"),
        P("ep", "tp", None),
        P(None, "tp"),
        P(None, "tp"),
        P("tp", None),
        P(),
    )
    return jax.shard_map(
        on_device, mesh=mesh, in_specs=placed, out_specs=P("ep", "tp"), check_vma=False
    )
```

```python
import jax
import jax.numpy as jnp
from jax import lax
from jax.sharding import PartitionSpec as P

HEAD = 128


def slots_of(block_routes, experts, capacity):
    length, picks = block_routes.shape
    count = length * picks
    flat = block_routes.reshape(count)
    onehot = flat[:, None] == jnp.arange(experts, dtype=jnp.int32)[None, :]
    places = jnp.arange(count, dtype=jnp.int32)
    earlier = (places[:, None] > places[None, :]).astype(jnp.bfloat16)
    before = jnp.dot(earlier, onehot.astype(jnp.bfloat16), preferred_element_type=jnp.float32)
    rank = jnp.sum(jnp.where(onehot, before, 0.0), axis=1).astype(jnp.int32)
    slot = flat * capacity + rank
    return slot.reshape(length, picks)


def attend_local(query_block, key_block, value_block, segment):
    length = query_block.shape[0]
    heads = query_block.shape[1] // HEAD
    places = jnp.arange(length, dtype=jnp.int32)
    allowed = (segment[:, None] == segment[None, :]) & (places[:, None] >= places[None, :])
    query_heads = query_block.reshape(length, heads, HEAD)
    key_heads = key_block.reshape(length, heads, HEAD)
    value_heads = value_block.reshape(length, heads, HEAD)
    scores = jnp.einsum(
        "qhd,khd->hqk", query_heads, key_heads, preferred_element_type=jnp.float32
    ) * HEAD ** (-0.5)
    scores = jnp.where(allowed[None], scores, -jnp.inf)
    highest = jnp.max(scores, axis=2, keepdims=True)
    weights = jnp.exp(scores - highest)
    shares = (weights / jnp.sum(weights, axis=2, keepdims=True)).astype(jnp.bfloat16)
    attended = jnp.einsum("hqk,khd->qhd", shares, value_heads, preferred_element_type=jnp.float32)
    return attended.astype(jnp.bfloat16).reshape(length, heads * HEAD)


def on_device(
    stream,
    queries,
    keys_in,
    values_in,
    segment_ids,
    routes,
    route_weights,
    w_out,
    norm_gain,
    expert_gate,
    expert_up,
    expert_down,
    shared_gate,
    shared_up,
    shared_down,
    shared_router,
):
    length, width = stream.shape
    ep_count = lax.axis_size("ep")
    tp_count = lax.axis_size("tp")
    attended = attend_local(queries, keys_in, values_in, segment_ids[0])
    partial_value = jnp.dot(attended, w_out, preferred_element_type=jnp.float32)
    summed_cols = lax.psum_scatter(
        partial_value.astype(jnp.bfloat16), "tp", scatter_dimension=1, tiled=True
    )
    summed = lax.all_gather(summed_cols, "tp", axis=1, tiled=True)
    resid = stream.astype(jnp.float32) + summed.astype(jnp.float32)
    normed = (
        resid * lax.rsqrt(jnp.mean(resid * resid, axis=1, keepdims=True) + 1e-06) * norm_gain
    ).astype(jnp.bfloat16)
    shared_gate_rows = jnp.dot(normed, shared_gate, preferred_element_type=jnp.float32)
    shared_up_rows = jnp.dot(normed, shared_up, preferred_element_type=jnp.float32)
    shared_hidden = (jax.nn.silu(shared_gate_rows) * shared_up_rows).astype(jnp.bfloat16)
    shared_part = jnp.dot(shared_hidden, shared_down, preferred_element_type=jnp.float32)
    shared_cols = lax.psum_scatter(
        shared_part.astype(jnp.bfloat16), "tp", scatter_dimension=1, tiled=True
    ).astype(jnp.float32)
    shared_scale = jax.nn.sigmoid(
        jnp.dot(normed, shared_router, preferred_element_type=jnp.float32)
    )
    local_experts = expert_gate.shape[0]
    experts = local_experts * ep_count
    picks = routes.shape[1]
    divisor = 2 * experts * tp_count
    capacity = tp_count * ((3 * length * picks + divisor - 1) // divisor)
    slot = slots_of(routes, experts, capacity)
    slot_ids = jnp.arange(experts * capacity, dtype=jnp.int32)
    hits = slot[:, :, None] == slot_ids[None, None, :]
    chosen = jnp.any(hits, axis=1).T.astype(jnp.bfloat16)
    chosen = chosen.reshape(ep_count, local_experts, capacity, length)
    slot_grid = (
        jnp.arange(ep_count, dtype=jnp.int32)[:, None, None] * local_experts
        + jnp.arange(local_experts, dtype=jnp.int32)[None, :, None]
    ) * capacity + jnp.arange(capacity, dtype=jnp.int32)[None, None, :]
    pieces = [(0, 0, capacity)] if local_experts < 2 else []
    for index in range(local_experts):
        if index == local_experts - 1 and capacity % 2 == 0 and local_experts > 1:
            pieces += [(index, 0, capacity // 2), (index, capacity // 2, capacity)]
        elif local_experts > 1:
            pieces.append((index, 0, capacity))
    mixes = []
    for index, first, last in pieces:
        ids = slot_grid[:, index, first:last].reshape(-1)
        hit = slot[:, :, None] == ids[None, None, :]
        mixing = jnp.sum(jnp.where(hit, route_weights[:, :, None], 0.0), axis=1)
        high = mixing.astype(jnp.bfloat16)
        low = (mixing - high.astype(jnp.float32)).astype(jnp.bfloat16)
        mixes.append((high, low))
    routed = None
    for index in range(local_experts):
        outgoing = jnp.einsum(
            "sct,td->scd", chosen[:, index], normed, preferred_element_type=jnp.float32
        ).astype(jnp.bfloat16)
        rows = lax.all_to_all(outgoing, "ep", split_axis=0, concat_axis=0, tiled=True)
        gate_rows = jnp.einsum(
            "scd,df->scf", rows, expert_gate[index], preferred_element_type=jnp.float32
        )
        up_rows = jnp.einsum(
            "scd,df->scf", rows, expert_up[index], preferred_element_type=jnp.float32
        )
        expert_hidden = (jax.nn.silu(gate_rows) * up_rows).astype(jnp.bfloat16)
        for place, (owner, first, last) in enumerate(pieces):
            if owner != index:
                continue
            expert_part = jnp.einsum(
                "scf,fd->scd",
                expert_hidden[:, first:last],
                expert_down[index],
                preferred_element_type=jnp.float32,
            ).astype(jnp.bfloat16)
            if place == len(pieces) - 2:
                expert_part, mixes = lax.optimization_barrier((expert_part, mixes))
            expert_cols = lax.psum_scatter(expert_part, "tp", scatter_dimension=2, tiled=True)
            returned = lax.all_to_all(expert_cols, "ep", split_axis=0, concat_axis=0, tiled=True)
            columns = returned.shape[2]
            flat_results = returned.reshape(-1, columns)
            high, low = mixes[place]
            term = jnp.dot(high, flat_results, preferred_element_type=jnp.float32) + jnp.dot(
                low, flat_results, preferred_element_type=jnp.float32
            )
            routed = term if routed is None else routed + term
    resid_cols = lax.dynamic_slice_in_dim(resid, lax.axis_index("tp") * columns, columns, 1)
    return (resid_cols + shared_scale[:, None] * shared_cols + routed).astype(jnp.bfloat16)


def solution(mesh):
    placed = (
        P("ep", None),
        P("ep", "tp"),
        P("ep", "tp"),
        P("ep", "tp"),
        P("ep", None),
        P("ep", None),
        P("ep", None),
        P("tp", None),
        P(),
        P("ep", None, "tp"),
        P("ep", None, "tp"),
        P("ep", "tp", None),
        P(None, "tp"),
        P(None, "tp"),
        P("tp", None),
        P(),
    )
    return jax.shard_map(
        on_device, mesh=mesh, in_specs=placed, out_specs=P("ep", "tp"), check_vma=False
    )
```

```python
import jax
import jax.numpy as jnp
from jax import lax
from jax.sharding import PartitionSpec as P

HEAD = 128


def slots_of(block_routes, experts, capacity):
    length, picks = block_routes.shape
    count = length * picks
    flat = block_routes.reshape(count)
    onehot = flat[:, None] == jnp.arange(experts, dtype=jnp.int32)[None, :]
    places = jnp.arange(count, dtype=jnp.int32)
    earlier = (places[:, None] > places[None, :]).astype(jnp.bfloat16)
    before = jnp.dot(earlier, onehot.astype(jnp.bfloat16), preferred_element_type=jnp.float32)
    rank = jnp.sum(jnp.where(onehot, before, 0.0), axis=1).astype(jnp.int32)
    slot = flat * capacity + rank
    return slot.reshape(length, picks)


def attend_local(query_block, key_block, value_block, segment):
    length = query_block.shape[0]
    heads = query_block.shape[1] // HEAD
    places = jnp.arange(length, dtype=jnp.int32)
    allowed = (segment[:, None] == segment[None, :]) & (places[:, None] >= places[None, :])
    query_heads = query_block.reshape(length, heads, HEAD)
    key_heads = key_block.reshape(length, heads, HEAD)
    value_heads = value_block.reshape(length, heads, HEAD)
    scores = jnp.einsum(
        "qhd,khd->hqk", query_heads, key_heads, preferred_element_type=jnp.float32
    ) * HEAD ** (-0.5)
    scores = jnp.where(allowed[None], scores, -jnp.inf)
    highest = jnp.max(scores, axis=2, keepdims=True)
    weights = jnp.exp(scores - highest)
    shares = (weights / jnp.sum(weights, axis=2, keepdims=True)).astype(jnp.bfloat16)
    attended = jnp.einsum("hqk,khd->qhd", shares, value_heads, preferred_element_type=jnp.float32)
    return attended.astype(jnp.bfloat16).reshape(length, heads * HEAD)


def on_device(
    stream,
    queries,
    keys_in,
    values_in,
    segment_ids,
    routes,
    route_weights,
    w_out,
    norm_gain,
    expert_gate,
    expert_up,
    expert_down,
    shared_gate,
    shared_up,
    shared_down,
    shared_router,
):
    length, width = stream.shape
    ep_count = lax.axis_size("ep")
    tp_count = lax.axis_size("tp")
    attended = attend_local(queries, keys_in, values_in, segment_ids[0])
    partial_value = jnp.dot(attended, w_out, preferred_element_type=jnp.float32)
    summed_cols = lax.psum_scatter(
        partial_value.astype(jnp.bfloat16), "tp", scatter_dimension=1, tiled=True
    )
    summed = lax.all_gather(summed_cols, "tp", axis=1, tiled=True)
    resid = stream.astype(jnp.float32) + summed.astype(jnp.float32)
    normed = (
        resid * lax.rsqrt(jnp.mean(resid * resid, axis=1, keepdims=True) + 1e-06) * norm_gain
    ).astype(jnp.bfloat16)
    shared_gate_rows = jnp.dot(normed, shared_gate, preferred_element_type=jnp.float32)
    shared_up_rows = jnp.dot(normed, shared_up, preferred_element_type=jnp.float32)
    shared_hidden = (jax.nn.silu(shared_gate_rows) * shared_up_rows).astype(jnp.bfloat16)
    shared_part = jnp.dot(shared_hidden, shared_down, preferred_element_type=jnp.float32)
    shared_cols = lax.psum_scatter(
        shared_part.astype(jnp.bfloat16), "tp", scatter_dimension=1, tiled=True
    ).astype(jnp.float32)
    shared_scale = jax.nn.sigmoid(
        jnp.dot(normed, shared_router, preferred_element_type=jnp.float32)
    )
    local_experts = expert_gate.shape[0]
    experts = local_experts * ep_count
    picks = routes.shape[1]
    divisor = 2 * experts * tp_count
    capacity = tp_count * ((3 * length * picks + divisor - 1) // divisor)
    slot = slots_of(routes, experts, capacity)
    slot_ids = jnp.arange(experts * capacity, dtype=jnp.int32)
    hits = slot[:, :, None] == slot_ids[None, None, :]
    chosen = jnp.any(hits, axis=1).T.astype(jnp.bfloat16)
    chosen = chosen.reshape(ep_count, local_experts, capacity, length)
    slot_grid = (
        jnp.arange(ep_count, dtype=jnp.int32)[:, None, None] * local_experts
        + jnp.arange(local_experts, dtype=jnp.int32)[None, :, None]
    ) * capacity + jnp.arange(capacity, dtype=jnp.int32)[None, None, :]
    split = capacity * 3 // 4 if capacity % 4 == 0 else capacity // 2
    pieces = []
    for index in range(local_experts):
        pieces += [(index, 0, split), (index, split, capacity)]
    mixes = []
    for index, first, last in pieces:
        ids = slot_grid[:, index, first:last].reshape(-1)
        hit = slot[:, :, None] == ids[None, None, :]
        mixing = jnp.sum(jnp.where(hit, route_weights[:, :, None], 0.0), axis=1)
        high = mixing.astype(jnp.bfloat16)
        low = (mixing - high.astype(jnp.float32)).astype(jnp.bfloat16)
        mixes.append((high, low))
    routed = None
    for index in range(local_experts):
        outgoing = jnp.einsum(
            "sct,td->scd", chosen[:, index], normed, preferred_element_type=jnp.float32
        ).astype(jnp.bfloat16)
        rows = lax.all_to_all(outgoing, "ep", split_axis=0, concat_axis=0, tiled=True)
        gate_rows = jnp.einsum(
            "scd,df->scf", rows, expert_gate[index], preferred_element_type=jnp.float32
        )
        up_rows = jnp.einsum(
            "scd,df->scf", rows, expert_up[index], preferred_element_type=jnp.float32
        )
        expert_hidden = (jax.nn.silu(gate_rows) * up_rows).astype(jnp.bfloat16)
        for place, (owner, first, last) in enumerate(pieces):
            if owner != index:
                continue
            expert_part = jnp.einsum(
                "scf,fd->scd",
                expert_hidden[:, first:last],
                expert_down[index],
                preferred_element_type=jnp.float32,
            ).astype(jnp.bfloat16)
            if place == len(pieces) - 2:
                expert_part, mixes = lax.optimization_barrier((expert_part, mixes))
            expert_cols = lax.psum_scatter(expert_part, "tp", scatter_dimension=2, tiled=True)
            returned = lax.all_to_all(expert_cols, "ep", split_axis=0, concat_axis=0, tiled=True)
            columns = returned.shape[2]
            flat_results = returned.reshape(-1, columns)
            high, low = mixes[place]
            term = jnp.dot(high, flat_results, preferred_element_type=jnp.float32) + jnp.dot(
                low, flat_results, preferred_element_type=jnp.float32
            )
            routed = term if routed is None else routed + term
    resid_cols = lax.dynamic_slice_in_dim(resid, lax.axis_index("tp") * columns, columns, 1)
    return (resid_cols + shared_scale[:, None] * shared_cols + routed).astype(jnp.bfloat16)


def solution(mesh):
    placed = (
        P("ep", None),
        P("ep", "tp"),
        P("ep", "tp"),
        P("ep", "tp"),
        P("ep", None),
        P("ep", None),
        P("ep", None),
        P("tp", None),
        P(),
        P("ep", None, "tp"),
        P("ep", None, "tp"),
        P("ep", "tp", None),
        P(None, "tp"),
        P(None, "tp"),
        P("tp", None),
        P(),
    )
    return jax.shard_map(
        on_device, mesh=mesh, in_specs=placed, out_specs=P("ep", "tp"), check_vma=False
    )
```
